256 devices in a mesh: row: 16 (over z, core), col: 16 (over y, x).
Axes of the slice: x: 4, y: 4, z: 8, core: 2. Of those that a mesh axis runs over, the one named last changes fastest.
Arguments:
- matrix: bfloat16 [4096, 262144], P('row', 'col'), may hold values from -60 to 60
- test_matrix: bfloat16 [262144, 512], P(('col', 'row')), may hold values from -0.0390625 to 0.0390625
Outputs:
- orthonormal: float32 [4096, 512], P(('row', 'col'))
- triangular: float32 [512, 512], replicated
The draws below stay inside these ranges and needn't reach their ends.
All inputs are finite; a program needn't handle non-finite values.
Results may differ from the reference program's by a relative error of at most 0.0003.
Values may be sent and summed in bfloat16 or wider, within the bound.
No kernel may reach another device: no remote copies, remote signals or barrier semaphores. Data moves between devices by JAX's collectives and lax.ppermute only.
A program may use at most 128 MiB of HBM per device.

```python
import jax
import jax.numpy as jnp
from jax import lax

K = 512
ROWS = 4096
COLS = 262144


def draw_matrix(key, part):
    first, second = jax.random.split(jax.random.fold_in(key, 11), 2)
    position = jnp.arange(ROWS, dtype=jnp.float32) / jnp.float32(ROWS)
    spread = jax.random.uniform(second, (ROWS, 1), dtype=jnp.float32)
    scales = 0.4 * 10.0 ** spread * 3.0 ** position[:, None]
    values = jnp.clip(jax.random.normal(first, (ROWS, COLS), dtype=jnp.float32), -5.0, 5.0)
    return (values * scales).astype(jnp.bfloat16)


def draw_test_matrix(key, part):
    first, second = jax.random.split(jax.random.fold_in(key, 23), 2)
    spread = jax.random.uniform(second, (1, K), dtype=jnp.float32)
    scales = 0.5 * 10.0 ** spread / jnp.sqrt(jnp.float32(COLS))
    values = jnp.clip(jax.random.normal(first, (COLS, K), dtype=jnp.float32), -4.0, 4.0)
    return (values * scales).astype(jnp.bfloat16)


def setup_inputs(seed: int = 0) -> dict:
    key_list = jax.random.split(jax.random.key(seed), 3)
    matrix = draw_matrix(jax.random.fold_in(key_list[2], 71), 0)
    test_matrix = draw_test_matrix(jax.random.fold_in(key_list[2], 71), 0)
    return dict(matrix=matrix, test_matrix=test_matrix)


def reference(matrix, test_matrix):
    sketch = jnp.dot(matrix.astype(jnp.float32), test_matrix.astype(jnp.float32), preferred_element_type=jnp.float32)
    total_rows = sketch.shape[0]
    gram = jnp.dot(sketch.T, sketch, precision=lax.Precision.HIGHEST) / jnp.float32(total_rows)
    lower_factor = jnp.linalg.cholesky(gram)
    orthonormal = lax.linalg.triangular_solve(lower_factor, sketch, left_side=False, lower=True, transpose_a=True)
    return (orthonormal, lower_factor.T)
```

```python
import jax
import jax.numpy as jnp
from jax import lax
from jax.sharding import PartitionSpec as P


def probe_product(matrix, test_matrix):
    return jnp.dot(
        matrix,
        lax.all_gather(test_matrix, "row", axis=0, tiled=True),
        preferred_element_type=jnp.float32,
    )


def scatter_sum(value, axis, parts):
    pieces = value.reshape(parts, value.shape[0] // parts, *value.shape[1:])
    return lax.all_to_all(pieces, axis, 0, 0, tiled=False).sum(0)


def gather_rows(value, axis, parts):
    copies = jnp.broadcast_to(value[None], (parts, *value.shape))
    gathered = lax.all_to_all(copies, axis, 0, 0, tiled=False)
    return gathered.reshape(parts * value.shape[0], *value.shape[1:])


def shards(matrix, test_matrix):
    n_col = lax.axis_size("col")
    n_row = lax.axis_size("row")
    total_rows = matrix.shape[0] * n_row
    k = test_matrix.shape[1]
    partial_value = probe_product(matrix, test_matrix)
    own_rows = scatter_sum(partial_value, "col", n_col)
    sketch = gather_rows(own_rows, "col", n_col)
    width = k // n_col
    col = lax.axis_index("col")
    columns = lax.dynamic_slice_in_dim(sketch, col * width, width, 1)
    gram_part = jnp.dot(sketch.T, columns, precision=lax.Precision.HIGHEST)
    gram_part = gather_rows(scatter_sum(gram_part, "row", n_row), "row", n_row)
    blocks = gather_rows(gram_part.T, "col", n_col)
    gram = blocks.T / jnp.float32(total_rows)
    lower_factor = jnp.linalg.cholesky(gram)
    orthonormal = lax.linalg.triangular_solve(
        lower_factor, own_rows, left_side=False, lower=True, transpose_a=True
    )
    return (orthonormal, lower_factor.T)


def solution(mesh):
    in_specs = (P("row", "col"), P(("col", "row"), None))
    out_specs = (P(("row", "col"), None), P())
    return jax.shard_map(shards, mesh=mesh, in_specs=in_specs, out_specs=out_specs, check_vma=False)
```

```python
import jax
import jax.numpy as jnp
from jax import lax
from jax.experimental import pallas as pl
from jax.experimental.pallas import tpu as pltpu
from jax.sharding import PartitionSpec as P

PANEL = 128


def factor_kernel(a_ref, r_ref, w_ref):
    n, width = a_ref.shape
    w_ref[...] = a_ref[...]
    for k in range(n // PANEL):
        base = k * PANEL
        lanes = lax.broadcasted_iota(jnp.int32, (1, width - base), 1) + base
        if base:
            r_ref[base:base + PANEL, :base] = jnp.zeros((PANEL, base), jnp.float32)

        def step(t, carry, base=base, lanes=lanes):
            j = base + t
            row = w_ref[pl.ds(j, 1), base:]
            pivot = jnp.sum(jnp.where(lanes == j, row, 0.0), axis=1, keepdims=True)
            scale = lax.rsqrt(pivot)
            scale = scale * (1.5 - 0.5 * pivot * scale * scale)
            top = jnp.where(lanes >= j, row * scale, 0.0)
            r_ref[pl.ds(j, 1), base:] = top
            head = jnp.broadcast_to(top[:, :PANEL], (8, PANEL))
            column = jnp.transpose(head)[:, 0:1]
            w_ref[base:base + PANEL, base:] = w_ref[base:base + PANEL, base:] - column * top
            return carry

        lax.fori_loop(0, PANEL, step, 0)
        rest = base + PANEL
        if rest < n:
            block = r_ref[base:rest, rest:]
            left = jnp.transpose(block[:, :n - rest])
            update = jnp.dot(left, block, precision=lax.Precision.HIGHEST, preferred_element_type=jnp.float32)
            w_ref[rest:n, rest:] = w_ref[rest:n, rest:] - update


def factor(augmented):
    n, width = augmented.shape
    return pl.pallas_call(
        factor_kernel,
        out_shape=jax.ShapeDtypeStruct((n, width), jnp.float32),
        in_specs=[pl.BlockSpec(memory_space=pltpu.VMEM)],
        out_specs=pl.BlockSpec(memory_space=pltpu.VMEM),
        scratch_shapes=[pltpu.VMEM((n, width), jnp.float32)],
    )(augmented)


def probe_product(matrix, test_matrix):
    return jnp.dot(
        matrix,
        lax.all_gather(test_matrix, "row", axis=0, tiled=True),
        preferred_element_type=jnp.float32,
    )


def scatter_sum(value, axis, parts):
    pieces = value.reshape(parts, value.shape[0] // parts, *value.shape[1:])
    return lax.all_to_all(pieces, axis, 0, 0, tiled=False).sum(0)


def gather_rows(value, axis, parts):
    copies = jnp.broadcast_to(value[None], (parts, *value.shape))
    gathered = lax.all_to_all(copies, axis, 0, 0, tiled=False)
    return gathered.reshape(parts * value.shape[0], *value.shape[1:])


def shards(matrix, test_matrix):
    n_col = lax.axis_size("col")
    n_row = lax.axis_size("row")
    total_rows = matrix.shape[0] * n_row
    k = test_matrix.shape[1]
    partial_value = probe_product(matrix, test_matrix)
    own_rows = scatter_sum(partial_value, "col", n_col)
    sketch = gather_rows(own_rows, "col", n_col)
    width = k // n_col
    col = lax.axis_index("col")
    columns = lax.dynamic_slice_in_dim(sketch, col * width, width, 1)
    gram_part = jnp.dot(sketch.T, columns, precision=lax.Precision.HIGHEST)
    gram_part = gather_rows(scatter_sum(gram_part, "row", n_row), "row", n_row)
    blocks = gather_rows(gram_part.T, "col", n_col)
    gram = blocks.T / jnp.float32(total_rows)
    share = own_rows.shape[0]
    pad = jnp.zeros((k, PANEL - share), jnp.float32)
    factored = factor(jnp.concatenate([gram, own_rows.T, pad], axis=1))
    return (factored[:, k:k + share].T, factored[:, :k])


def solution(mesh):
    in_specs = (P("row", "col"), P(("col", "row"), None))
    out_specs = (P(("row", "col"), None), P())
    return jax.shard_map(shards, mesh=mesh, in_specs=in_specs, out_specs=out_specs, check_vma=False)
```

```python
import jax
import jax.numpy as jnp
from jax import lax
from jax.experimental import pallas as pl
from jax.experimental.pallas import tpu as pltpu
from jax.sharding import PartitionSpec as P

PANEL = 128
GROUP = 8


def factor_kernel(a_ref, r_ref, w_ref, head_ref):
    n, width = a_ref.shape
    w_ref[...] = a_ref[...]
    head_ref[...] = jnp.zeros(head_ref.shape, jnp.float32)
    subl = lax.broadcasted_iota(jnp.int32, (GROUP, 1), 0)
    for k in range(n // PANEL):
        base = k * PANEL
        span = width - base
        lanes = lax.broadcasted_iota(jnp.int32, (GROUP, span), 1) + base
        if base:
            r_ref[base:base + PANEL, :base] = jnp.zeros((PANEL, base), jnp.float32)

        def group(g, carry, base=base, span=span, lanes=lanes):
            r0 = pl.multiple_of(base + g * GROUP, GROUP)
            block = w_ref[pl.ds(r0, GROUP), base:]
            rows = jnp.zeros((GROUP, span), jnp.float32)
            for t in range(GROUP):
                j = r0 + t
                column = jnp.sum(jnp.where(lanes[:, :PANEL] == j, block[:, :PANEL], 0.0), axis=1, keepdims=True)
                pivot = column[t:t + 1, :]
                scale = lax.rsqrt(pivot)
                scale = scale * (1.5 - 0.5 * pivot * scale * scale)
                top = jnp.where(lanes[:1] >= j, block[t:t + 1, :] * scale, 0.0)
                rows = jnp.where(subl == t, top, rows)
                factor_col = jnp.where(subl > t, column * scale, 0.0)
                block = block - factor_col * top
            r_ref[pl.ds(r0, GROUP), base:] = rows
            head_ref[:, :GROUP] = jnp.transpose(rows[:, :PANEL])[:, :GROUP]

            def slab(s, c):
                at = pl.multiple_of(base + s * GROUP, GROUP)
                part = w_ref[pl.ds(at, GROUP), base:]
                mult = head_ref[pl.ds(pl.multiple_of(s * GROUP, GROUP), GROUP), :]
                for t in range(GROUP):
                    part = part - mult[:, t:t + 1] * rows[t:t + 1, :]
                w_ref[pl.ds(at, GROUP), base:] = part
                return c

            lax.fori_loop(g + 1, PANEL // GROUP, slab, 0)
            return carry

        lax.fori_loop(0, PANEL // GROUP, group, 0)
        rest = base + PANEL
        if rest < n:
            block = r_ref[base:rest, rest:]
            left = jnp.transpose(block[:, :n - rest])
            update = jnp.dot(left, block, precision=lax.Precision.HIGHEST, preferred_element_type=jnp.float32)
            w_ref[rest:n, rest:] = w_ref[rest:n, rest:] - update


def factor(augmented):
    n, width = augmented.shape
    return pl.pallas_call(
        factor_kernel,
        out_shape=jax.ShapeDtypeStruct((n, width), jnp.float32),
        in_specs=[pl.BlockSpec(memory_space=pltpu.VMEM)],
        out_specs=pl.BlockSpec(memory_space=pltpu.VMEM),
        scratch_shapes=[pltpu.VMEM((n, width), jnp.float32), pltpu.VMEM((PANEL, PANEL), jnp.float32)],
    )(augmented)


def probe_product(matrix, test_matrix):
    return jnp.dot(
        matrix,
        lax.all_gather(test_matrix, "row", axis=0, tiled=True),
        preferred_element_type=jnp.float32,
    )


def scatter_sum(value, axis, parts):
    pieces = value.reshape(parts, value.shape[0] // parts, *value.shape[1:])
    return lax.all_to_all(pieces, axis, 0, 0, tiled=False).sum(0)


def gather_rows(value, axis, parts):
    copies = jnp.broadcast_to(value[None], (parts, *value.shape))
    gathered = lax.all_to_all(copies, axis, 0, 0, tiled=False)
    return gathered.reshape(parts * value.shape[0], *value.shape[1:])


def shards(matrix, test_matrix):
    n_col = lax.axis_size("col")
    n_row = lax.axis_size("row")
    total_rows = matrix.shape[0] * n_row
    k = test_matrix.shape[1]
    partial_value = probe_product(matrix, test_matrix)
    own_rows = scatter_sum(partial_value, "col", n_col)
    sketch = gather_rows(own_rows, "col", n_col)
    width = k // n_col
    col = lax.axis_index("col")
    columns = lax.dynamic_slice_in_dim(sketch, col * width, width, 1)
    gram_part = jnp.dot(sketch.T, columns, precision=lax.Precision.HIGHEST)
    gram_part = gather_rows(scatter_sum(gram_part, "row", n_row), "row", n_row)
    blocks = gather_rows(gram_part.T, "col", n_col)
    gram = blocks.T / jnp.float32(total_rows)
    share = own_rows.shape[0]
    pad = jnp.zeros((k, PANEL - share), jnp.float32)
    factored = factor(jnp.concatenate([gram, own_rows.T, pad], axis=1))
    return (factored[:, k:k + share].T, factored[:, :k])


def solution(mesh):
    in_specs = (P("row", "col"), P(("col", "row"), None))
    out_specs = (P(("row", "col"), None), P())
    return jax.shard_map(shards, mesh=mesh, in_specs=in_specs, out_specs=out_specs, check_vma=False)
```

```python
import jax
import jax.numpy as jnp
from jax import lax
from jax.experimental import pallas as pl
from jax.experimental.pallas import tpu as pltpu
from jax.sharding import PartitionSpec as P

PANEL = 128
GROUP = 8


def factor_kernel(a_ref, r_ref, w_ref, head_ref, row_ref):
    n, width = a_ref.shape
    w_ref[...] = a_ref[...]
    subl = lax.broadcasted_iota(jnp.int32, (GROUP, 1), 0)
    for k in range(n // PANEL):
        base = k * PANEL
        span = width - base
        lanes = lax.broadcasted_iota(jnp.int32, (GROUP, span), 1) + base
        if base:
            r_ref[base:base + PANEL, :base] = jnp.zeros((PANEL, base), jnp.float32)

        def group(g, carry, base=base, span=span, lanes=lanes):
            r0 = pl.multiple_of(base + g * GROUP, GROUP)
            block = w_ref[pl.ds(r0, GROUP), base:]
            rows = jnp.zeros((GROUP, span), jnp.float32)
            for t in range(GROUP):
                j = r0 + t
                column = jnp.sum(jnp.where(lanes[:, :PANEL] == j, block[:, :PANEL], 0.0), axis=1, keepdims=True)
                pivot = column[t:t + 1, :]
                scale = lax.rsqrt(pivot)
                scale = scale * (1.5 - 0.5 * pivot * scale * scale)
                top = jnp.where(lanes[:1] >= j, block[t:t + 1, :] * scale, 0.0)
                rows = jnp.where(subl == t, top, rows)
                factor_col = jnp.where(subl > t, column * scale, 0.0)
                block = block - factor_col * top
            r_ref[pl.ds(r0, GROUP), base:] = rows
            head = jnp.transpose(rows[:, :PANEL])
            for t in range(GROUP):
                row_ref[t, :, :span] = jnp.broadcast_to(rows[t:t + 1, :], (GROUP, span))
                head_ref[t] = jnp.broadcast_to(head[:, t:t + 1], (PANEL, PANEL))

            def slab(s, c):
                at = pl.multiple_of(base + s * GROUP, GROUP)
                off = pl.multiple_of(s * GROUP, GROUP)
                part = w_ref[pl.ds(at, GROUP), base:]
                for t in range(GROUP):
                    mult = head_ref[t, pl.ds(off, GROUP), :]
                    mult = jnp.concatenate([mult] * (span // PANEL), axis=1)
                    part = part - mult * row_ref[t, :, :span]
                w_ref[pl.ds(at, GROUP), base:] = part
                return c

            lax.fori_loop(g + 1, PANEL // GROUP, slab, 0)
            return carry

        lax.fori_loop(0, PANEL // GROUP, group, 0)
        rest = base + PANEL
        if rest < n:
            block = r_ref[base:rest, rest:]
            left = jnp.transpose(block[:, :n - rest])
            update = jnp.dot(left, block, precision=lax.Precision.HIGHEST, preferred_element_type=jnp.float32)
            w_ref[rest:n, rest:] = w_ref[rest:n, rest:] - update


def factor(augmented):
    n, width = augmented.shape
    return pl.pallas_call(
        factor_kernel,
        out_shape=jax.ShapeDtypeStruct((n, width), jnp.float32),
        in_specs=[pl.BlockSpec(memory_space=pltpu.VMEM)],
        out_specs=pl.BlockSpec(memory_space=pltpu.VMEM),
        scratch_shapes=[
            pltpu.VMEM((n, width), jnp.float32),
            pltpu.VMEM((GROUP, PANEL, PANEL), jnp.float32),
            pltpu.VMEM((GROUP, GROUP, width), jnp.float32),
        ],
    )(augmented)


def probe_product(matrix, test_matrix):
    return jnp.dot(
        matrix,
        lax.all_gather(test_matrix, "row", axis=0, tiled=True),
        preferred_element_type=jnp.float32,
    )


def scatter_sum(value, axis, parts):
    pieces = value.reshape(parts, value.shape[0] // parts, *value.shape[1:])
    return lax.all_to_all(pieces, axis, 0, 0, tiled=False).sum(0)


def gather_rows(value, axis, parts):
    copies = jnp.broadcast_to(value[None], (parts, *value.shape))
    gathered = lax.all_to_all(copies, axis, 0, 0, tiled=False)
    return gathered.reshape(parts * value.shape[0], *value.shape[1:])


def shards(matrix, test_matrix):
    n_col = lax.axis_size("col")
    n_row = lax.axis_size("row")
    total_rows = matrix.shape[0] * n_row
    k = test_matrix.shape[1]
    partial_value = probe_product(matrix, test_matrix)
    own_rows = scatter_sum(partial_value, "col", n_col)
    sketch = gather_rows(own_rows, "col", n_col)
    width = k // n_col
    col = lax.axis_index("col")
    columns = lax.dynamic_slice_in_dim(sketch, col * width, width, 1)
    gram_part = jnp.dot(sketch.T, columns, precision=lax.Precision.HIGHEST)
    gram_part = gather_rows(scatter_sum(gram_part, "row", n_row), "row", n_row)
    blocks = gather_rows(gram_part.T, "col", n_col)
    gram = blocks.T / jnp.float32(total_rows)
    share = own_rows.shape[0]
    pad = jnp.zeros((k, PANEL - share), jnp.float32)
    factored = factor(jnp.concatenate([gram, own_rows.T, pad], axis=1))
    return (factored[:, k:k + share].T, factored[:, :k])


def solution(mesh):
    in_specs = (P("row", "col"), P(("col", "row"), None))
    out_specs = (P(("row", "col"), None), P())
    return jax.shard_map(shards, mesh=mesh, in_specs=in_specs, out_specs=out_specs, check_vma=False)
```

```python
import jax
import jax.numpy as jnp
from jax import lax
from jax.experimental import pallas as pl
from jax.experimental.pallas import tpu as pltpu
from jax.sharding import PartitionSpec as P

PANEL = 128
CHUNKS = 2
GROUP = 8


def factor_kernel(a_ref, r_ref, w_ref, head_ref, row_ref):
    n, width = a_ref.shape
    w_ref[...] = a_ref[...]
    subl = lax.broadcasted_iota(jnp.int32, (GROUP, 1), 0)
    for k in range(n // PANEL):
        base = k * PANEL
        span = width - base
        lanes = lax.broadcasted_iota(jnp.int32, (GROUP, span), 1) + base
        if base:
            r_ref[base:base + PANEL, :base] = jnp.zeros((PANEL, base), jnp.float32)

        def group(g, carry, base=base, span=span, lanes=lanes):
            r0 = pl.multiple_of(base + g * GROUP, GROUP)
            block = w_ref[pl.ds(r0, GROUP), base:]
            rows = jnp.zeros((GROUP, span), jnp.float32)
            for t in range(GROUP):
                j = r0 + t
                column = jnp.sum(jnp.where(lanes[:, :PANEL] == j, block[:, :PANEL], 0.0), axis=1, keepdims=True)
                pivot = column[t:t + 1, :]
                scale = lax.rsqrt(pivot)
                scale = scale * (1.5 - 0.5 * pivot * scale * scale)
                top = jnp.where(lanes[:1] >= j, block[t:t + 1, :] * scale, 0.0)
                rows = jnp.where(subl == t, top, rows)
                factor_col = jnp.where(subl > t, column * scale, 0.0)
                block = block - factor_col * top
            r_ref[pl.ds(r0, GROUP), base:] = rows
            head = jnp.transpose(rows[:, :PANEL])
            for t in range(GROUP):
                row_ref[t, :, :span] = jnp.broadcast_to(rows[t:t + 1, :], (GROUP, span))
                head_ref[t] = jnp.broadcast_to(head[:, t:t + 1], (PANEL, PANEL))

            def slab(s, c):
                at = pl.multiple_of(base + s * GROUP, GROUP)
                off = pl.multiple_of(s * GROUP, GROUP)
                part = w_ref[pl.ds(at, GROUP), base:]
                for t in range(GROUP):
                    mult = head_ref[t, pl.ds(off, GROUP), :]
                    mult = jnp.concatenate([mult] * (span // PANEL), axis=1)
                    part = part - mult * row_ref[t, :, :span]
                w_ref[pl.ds(at, GROUP), base:] = part
                return c

            lax.fori_loop(g + 1, PANEL // GROUP, slab, 0)
            return carry

        lax.fori_loop(0, PANEL // GROUP, group, 0)
        rest = base + PANEL
        if rest < n:
            block = r_ref[base:rest, rest:]
            left = jnp.transpose(block[:, :n - rest])
            update = jnp.dot(left, block, precision=lax.Precision.HIGHEST, preferred_element_type=jnp.float32)
            w_ref[rest:n, rest:] = w_ref[rest:n, rest:] - update


def factor(augmented):
    n, width = augmented.shape
    return pl.pallas_call(
        factor_kernel,
        out_shape=jax.ShapeDtypeStruct((n, width), jnp.float32),
        in_specs=[pl.BlockSpec(memory_space=pltpu.VMEM)],
        out_specs=pl.BlockSpec(memory_space=pltpu.VMEM),
        scratch_shapes=[
            pltpu.VMEM((n, width), jnp.float32),
            pltpu.VMEM((GROUP, PANEL, PANEL), jnp.float32),
            pltpu.VMEM((GROUP, GROUP, width), jnp.float32),
        ],
    )(augmented)


def probe_product(matrix, test_matrix):
    return jnp.dot(
        matrix,
        lax.all_gather(test_matrix, "row", axis=0, tiled=True),
        preferred_element_type=jnp.float32,
    )


def scatter_sum(value, axis, parts):
    pieces = value.reshape(parts, value.shape[0] // parts, *value.shape[1:])
    return lax.all_to_all(pieces, axis, 0, 0, tiled=False).sum(0)


def gather_rows(value, axis, parts):
    copies = jnp.broadcast_to(value[None], (parts, *value.shape))
    gathered = lax.all_to_all(copies, axis, 0, 0, tiled=False)
    return gathered.reshape(parts * value.shape[0], *value.shape[1:])


def shards(matrix, test_matrix):
    n_col = lax.axis_size("col")
    n_row = lax.axis_size("row")
    total_rows = matrix.shape[0] * n_row
    k = test_matrix.shape[1]
    step = k // CHUNKS
    own_parts, sketch_parts = [], []
    for h in range(CHUNKS):
        partial_value = probe_product(matrix, test_matrix[:, h * step:(h + 1) * step])
        own_part = scatter_sum(partial_value, "col", n_col)
        own_parts.append(own_part)
        sketch_parts.append(gather_rows(own_part, "col", n_col))
    own_rows = jnp.concatenate(own_parts, axis=1)
    sketch = jnp.concatenate(sketch_parts, axis=1)
    width = k // n_col
    col = lax.axis_index("col")
    columns = lax.dynamic_slice_in_dim(sketch, col * width, width, 1)
    gram_part = jnp.dot(sketch.T, columns, precision=lax.Precision.HIGHEST)
    gram_part = gather_rows(scatter_sum(gram_part, "row", n_row), "row", n_row)
    blocks = gather_rows(gram_part.T, "col", n_col)
    gram = blocks.T / jnp.float32(total_rows)
    share = own_rows.shape[0]
    pad = jnp.zeros((k, PANEL - share), jnp.float32)
    factored = factor(jnp.concatenate([gram, own_rows.T, pad], axis=1))
    return (factored[:, k:k + share].T, factored[:, :k])


def solution(mesh):
    in_specs = (P("row", "col"), P(("col", "row"), None))
    out_specs = (P(("row", "col"), None), P())
    return jax.shard_map(shards, mesh=mesh, in_specs=in_specs, out_specs=out_specs, check_vma=False)
```

```python
import jax
import jax.numpy as jnp
from jax import lax
from jax.experimental import pallas as pl
from jax.experimental.pallas import tpu as pltpu
from jax.sharding import PartitionSpec as P

PANEL = 128
GROUP = 32


def factor_kernel(a_ref, e_ref, r_ref, x_ref, w_ref, head_ref, row_ref):
    n = a_ref.shape[0]
    width = n + e_ref.shape[1]
    w_ref[:, :n] = a_ref[...]
    w_ref[:, n:] = e_ref[...]
    subl = lax.broadcasted_iota(jnp.int32, (GROUP, 1), 0)
    tile = lax.broadcasted_iota(jnp.int32, (1, PANEL), 1)
    for k in range(n // PANEL):
        base = k * PANEL
        span = width - base
        lanes = lax.broadcasted_iota(jnp.int32, (GROUP, span), 1) + base
        if base:
            r_ref[base:base + PANEL, :base] = jnp.zeros((PANEL, base), jnp.float32)

        def group(g, carry, base=base, span=span, lanes=lanes):
            r0 = pl.multiple_of(base + g * GROUP, GROUP)
            block = w_ref[pl.ds(r0, GROUP), base:]
            diag = pltpu.roll(block[:, :PANEL], (PANEL - g * GROUP) % PANEL, 1)
            rows = jnp.zeros((GROUP, span), jnp.float32)
            for t in range(GROUP):
                j = r0 + t
                column = diag[:, t:t + 1]
                pivot = column[t:t + 1, :]
                scale = lax.rsqrt(pivot)
                scale = scale * (1.5 - 0.5 * pivot * scale * scale)
                factor_col = jnp.where(subl > t, column * scale, 0.0)
                near = jnp.where(tile >= t, diag[t:t + 1, :] * scale, 0.0)
                diag = diag - factor_col * near
                top = jnp.where(lanes[:1] >= j, block[t:t + 1, :] * scale, 0.0)
                rows = jnp.where(subl == t, top, rows)
                block = block - factor_col * top
            r_ref[pl.ds(r0, GROUP), base:] = rows[:, :n - base]
            x_ref[pl.ds(r0, GROUP), :] = rows[:, n - base:]
            head = jnp.transpose(rows[:, :PANEL])
            for t in range(GROUP):
                row_ref[t, :, :span] = jnp.broadcast_to(rows[t:t + 1, :], (GROUP, span))
                head_ref[t] = jnp.broadcast_to(head[:, t:t + 1], (PANEL, PANEL))

            def slab(s, c):
                at = pl.multiple_of(base + s * GROUP, GROUP)
                off = pl.multiple_of(s * GROUP, GROUP)
                part = w_ref[pl.ds(at, GROUP), base:]
                for t in range(GROUP):
                    mult = head_ref[t, pl.ds(off, GROUP), :]
                    mult = jnp.concatenate([mult] * (span // PANEL), axis=1)
                    part = part - mult * row_ref[t, :, :span]
                w_ref[pl.ds(at, GROUP), base:] = part
                return c

            lax.fori_loop(g + 1, PANEL // GROUP, slab, 0)
            return carry

        lax.fori_loop(0, PANEL // GROUP, group, 0)
        rest = base + PANEL
        if rest < n:
            left = r_ref[base:rest, rest:]
            block = jnp.concatenate([left, x_ref[base:rest, :]], axis=1)
            left = jnp.transpose(left)
            update = jnp.dot(left, block, precision=lax.Precision.HIGHEST, preferred_element_type=jnp.float32)
            w_ref[rest:n, rest:] = w_ref[rest:n, rest:] - update


def factor(gram, extra):
    n, more = gram.shape[0], extra.shape[1]
    width = n + more
    return pl.pallas_call(
        factor_kernel,
        out_shape=(jax.ShapeDtypeStruct((n, n), jnp.float32), jax.ShapeDtypeStruct((n, more), jnp.float32)),
        in_specs=[pl.BlockSpec(memory_space=pltpu.VMEM)] * 2,
        out_specs=(pl.BlockSpec(memory_space=pltpu.VMEM),) * 2,
        scratch_shapes=[
            pltpu.VMEM((n, width), jnp.float32),
            pltpu.VMEM((GROUP, PANEL, PANEL), jnp.float32),
            pltpu.VMEM((GROUP, GROUP, width), jnp.float32),
        ],
    )(gram, extra)


def probe_product(matrix, test_matrix):
    return jnp.dot(
        matrix,
        lax.all_gather(test_matrix, "row", axis=0, tiled=True),
        preferred_element_type=jnp.float32,
    )


def scatter_sum(value, axis, parts):
    pieces = value.reshape(parts, value.shape[0] // parts, *value.shape[1:])
    return lax.all_to_all(pieces, axis, 0, 0, tiled=False).sum(0)


def gather_rows(value, axis, parts):
    copies = jnp.broadcast_to(value[None], (parts, *value.shape))
    gathered = lax.all_to_all(copies, axis, 0, 0, tiled=False)
    return gathered.reshape(parts * value.shape[0], *value.shape[1:])


def shards(matrix, test_matrix):
    n_col = lax.axis_size("col")
    n_row = lax.axis_size("row")
    total_rows = matrix.shape[0] * n_row
    k = test_matrix.shape[1]
    partial_value = probe_product(matrix, test_matrix)
    own_rows = scatter_sum(partial_value, "col", n_col)
    sketch = gather_rows(own_rows, "col", n_col)
    width = k // n_col
    col = lax.axis_index("col")
    columns = lax.dynamic_slice_in_dim(sketch, col * width, width, 1)
    gram_part = jnp.dot(sketch.T, columns, precision=lax.Precision.HIGHEST)
    gram_part = gather_rows(scatter_sum(gram_part, "row", n_row), "row", n_row)
    gram = gather_rows(gram_part.T, "col", n_col) / jnp.float32(total_rows)
    share = own_rows.shape[0]
    extra = jnp.concatenate([own_rows.T, jnp.zeros((k, PANEL - share), jnp.float32)], axis=1)
    upper, solved = factor(gram, extra)
    return (solved[:, :share].T, upper)


def solution(mesh):
    in_specs = (P("row", "col"), P(("col", "row"), None))
    out_specs = (P(("row", "col"), None), P())
    return jax.shard_map(shards, mesh=mesh, in_specs=in_specs, out_specs=out_specs, check_vma=False)
```

```python
import jax
import jax.numpy as jnp
from jax import lax
from jax.experimental import pallas as pl
from jax.experimental.pallas import tpu as pltpu
from jax.sharding import PartitionSpec as P

PANEL = 128
GROUP = 32


def factor_kernel(a_ref, e_ref, r_ref, x_ref, w_ref, head_ref, row_ref):
    n = a_ref.shape[0]
    width = n + e_ref.shape[1]
    w_ref[:, :n] = a_ref[...]
    w_ref[:, n:] = e_ref[...]
    subl = lax.broadcasted_iota(jnp.int32, (GROUP, 1), 0)
    for k in range(n // PANEL):
        base = k * PANEL
        span = width - base
        lanes = lax.broadcasted_iota(jnp.int32, (1, span), 1) + base
        if base:
            r_ref[base:base + PANEL, :base] = jnp.zeros((PANEL, base), jnp.float32)
        for g in range(PANEL // GROUP):
            r0 = base + g * GROUP
            block = w_ref[r0:r0 + GROUP, base:]
            rows = jnp.zeros((GROUP, span), jnp.float32)
            for t in range(GROUP):
                j = r0 + t
                column = block[:, j - base:j - base + 1]
                pivot = column[t:t + 1, :]
                scale = lax.rsqrt(pivot)
                factor_col = jnp.where(subl > t, column * scale, 0.0)
                top = jnp.where(lanes >= j, block[t:t + 1, :] * scale, 0.0)
                rows = jnp.where(subl == t, top, rows)
                block = block - factor_col * top
            r_ref[r0:r0 + GROUP, base:] = rows[:, :n - base]
            x_ref[r0:r0 + GROUP, :] = rows[:, n - base:]
            below = r0 + GROUP - base
            if below < PANEL:
                head = jnp.transpose(rows[:, :PANEL])
                for t in range(GROUP):
                    row_ref[t, :, :span] = jnp.broadcast_to(rows[t:t + 1, :], (GROUP, span))
                    head_ref[t, below:, :] = jnp.broadcast_to(head[below:, t:t + 1], (PANEL - below, PANEL))
                for at in range(below, PANEL, GROUP):
                    part = w_ref[base + at:base + at + GROUP, base:]
                    for t in range(GROUP):
                        mult = head_ref[t, at:at + GROUP, :]
                        mult = jnp.concatenate([mult] * (span // PANEL), axis=1)
                        part = part - mult * row_ref[t, :, :span]
                    w_ref[base + at:base + at + GROUP, base:] = part
        rest = base + PANEL
        if rest < n:
            left = r_ref[base:rest, rest:]
            block = jnp.concatenate([left, x_ref[base:rest, :]], axis=1)
            left = jnp.transpose(left)
            update = jnp.dot(left, block, precision=lax.Precision.HIGHEST, preferred_element_type=jnp.float32)
            w_ref[rest:n, rest:] = w_ref[rest:n, rest:] - update


def factor(gram, extra):
    n, more = gram.shape[0], extra.shape[1]
    width = n + more
    return pl.pallas_call(
        factor_kernel,
        out_shape=(jax.ShapeDtypeStruct((n, n), jnp.float32), jax.ShapeDtypeStruct((n, more), jnp.float32)),
        in_specs=[pl.BlockSpec(memory_space=pltpu.VMEM)] * 2,
        out_specs=(pl.BlockSpec(memory_space=pltpu.VMEM),) * 2,
        scratch_shapes=[
            pltpu.VMEM((n, width), jnp.float32),
            pltpu.VMEM((GROUP, PANEL, PANEL), jnp.float32),
            pltpu.VMEM((GROUP, GROUP, width), jnp.float32),
        ],
    )(gram, extra)


def probe_product(matrix, test_matrix):
    return jnp.dot(
        matrix,
        lax.all_gather(test_matrix, "row", axis=0, tiled=True),
        preferred_element_type=jnp.float32,
    )


def scatter_sum(value, axis, parts):
    pieces = value.reshape(parts, value.shape[0] // parts, *value.shape[1:])
    return lax.all_to_all(pieces, axis, 0, 0, tiled=False).sum(0)


def gather_rows(value, axis, parts):
    copies = jnp.broadcast_to(value[None], (parts, *value.shape))
    gathered = lax.all_to_all(copies, axis, 0, 0, tiled=False)
    return gathered.reshape(parts * value.shape[0], *value.shape[1:])


def shards(matrix, test_matrix):
    n_col = lax.axis_size("col")
    n_row = lax.axis_size("row")
    total_rows = matrix.shape[0] * n_row
    k = test_matrix.shape[1]
    partial_value = probe_product(matrix, test_matrix)
    own_rows = scatter_sum(partial_value, "col", n_col)
    sketch = gather_rows(own_rows, "col", n_col)
    width = k // n_col
    col = lax.axis_index("col")
    columns = lax.dynamic_slice_in_dim(sketch, col * width, width, 1)
    gram_part = jnp.dot(sketch.T, columns, precision=lax.Precision.HIGHEST) / jnp.float32(total_rows)
    gram_part = gather_rows(scatter_sum(gram_part, "row", n_row), "row", n_row)
    gram = gather_rows(gram_part.T, "col", n_col)
    share = own_rows.shape[0]
    extra = jnp.concatenate([own_rows.T, jnp.zeros((k, PANEL - share), jnp.float32)], axis=1)
    upper, solved = factor(gram, extra)
    return (solved[:, :share].T, upper)


def solution(mesh):
    in_specs = (P("row", "col"), P(("col", "row"), None))
    out_specs = (P(("row", "col"), None), P())
    return jax.shard_map(shards, mesh=mesh, in_specs=in_specs, out_specs=out_specs, check_vma=False)
```

```python
import jax
import jax.numpy as jnp
from jax import lax
from jax.experimental import pallas as pl
from jax.experimental.pallas import tpu as pltpu
from jax.sharding import PartitionSpec as P

PANEL = 128
GROUP = 32


def factor_kernel(a_ref, e_ref, r_ref, x_ref, w_ref, head_ref, row_ref):
    n = a_ref.shape[0]
    width = n + e_ref.shape[1]
    w_ref[:, :n] = a_ref[...]
    w_ref[:, n:] = e_ref[...]
    subl = lax.broadcasted_iota(jnp.int32, (GROUP, 1), 0)
    for k in range(n // PANEL):
        base = k * PANEL
        span = width - base
        lanes = lax.broadcasted_iota(jnp.int32, (1, span), 1) + base
        if base:
            r_ref[base:base + PANEL, :base] = jnp.zeros((PANEL, base), jnp.float32)
        for g in range(PANEL // GROUP):
            r0 = base + g * GROUP
            block = w_ref[r0:r0 + GROUP, base:]
            rows = jnp.zeros((GROUP, span), jnp.float32)
            for t in range(GROUP):
                j = r0 + t
                column = block[:, j - base:j - base + 1]
                pivot = column[t:t + 1, :]
                scale = lax.rsqrt(pivot)
                factor_col = jnp.where(subl > t, column * scale, 0.0)
                top = jnp.where(lanes >= j, block[t:t + 1, :] * scale, 0.0)
                rows = jnp.where(subl == t, top, rows)
                block = block - factor_col * top
            r_ref[r0:r0 + GROUP, base:] = rows[:, :n - base]
            x_ref[r0:r0 + GROUP, :] = rows[:, n - base:]
            below = r0 + GROUP - base
            if below < PANEL:
                head = jnp.transpose(rows[:, :PANEL])
                for t in range(GROUP):
                    row_ref[t, :, :span] = jnp.broadcast_to(rows[t:t + 1, :], (GROUP, span))
                    head_ref[t, below:, :] = jnp.broadcast_to(head[below:, t:t + 1], (PANEL - below, PANEL))
                for at in range(below, PANEL, GROUP):
                    part = w_ref[base + at:base + at + GROUP, base:]
                    for t in range(GROUP):
                        mult = head_ref[t, at:at + GROUP, :]
                        mult = jnp.concatenate([mult] * (span // PANEL), axis=1)
                        part = part - mult * row_ref[t, :, :span]
                    w_ref[base + at:base + at + GROUP, base:] = part
        rest = base + PANEL
        if rest < n:
            left = r_ref[base:rest, rest:]
            block = jnp.concatenate([left, x_ref[base:rest, :]], axis=1)
            left = jnp.transpose(left)
            update = jnp.dot(left, block, precision=lax.Precision.HIGHEST, preferred_element_type=jnp.float32)
            w_ref[rest:n, rest:] = w_ref[rest:n, rest:] - update


def factor(gram, extra):
    n, more = gram.shape[0], extra.shape[1]
    width = n + more
    return pl.pallas_call(
        factor_kernel,
        out_shape=(jax.ShapeDtypeStruct((n, n), jnp.float32), jax.ShapeDtypeStruct((n, more), jnp.float32)),
        in_specs=[pl.BlockSpec(memory_space=pltpu.VMEM)] * 2,
        out_specs=(pl.BlockSpec(memory_space=pltpu.VMEM),) * 2,
        scratch_shapes=[
            pltpu.VMEM((n, width), jnp.float32),
            pltpu.VMEM((GROUP, PANEL, PANEL), jnp.float32),
            pltpu.VMEM((GROUP, GROUP, width), jnp.float32),
        ],
    )(gram, extra)


def probe_product(matrix, test_matrix):
    return jnp.dot(
        matrix,
        lax.all_gather(test_matrix, "row", axis=0, tiled=True),
        preferred_element_type=jnp.float32,
    )


def scatter_sum(value, axis, parts):
    pieces = value.reshape(parts, value.shape[0] // parts, *value.shape[1:])
    return lax.all_to_all(pieces, axis, 0, 0, tiled=False).sum(0)


def gather_rows(value, axis, parts):
    copies = jnp.broadcast_to(value[None], (parts, *value.shape))
    gathered = lax.all_to_all(copies, axis, 0, 0, tiled=False)
    return gathered.reshape(parts * value.shape[0], *value.shape[1:])


def butterfly_sum(value, axis, parts):
    assert parts & (parts - 1) == 0
    distance = 1
    while distance < parts:
        value = value + lax.ppermute(value, axis, [(i, i ^ distance) for i in range(parts)])
        distance *= 2
    return value


def shards(matrix, test_matrix):
    n_col = lax.axis_size("col")
    n_row = lax.axis_size("row")
    total_rows = matrix.shape[0] * n_row
    k = test_matrix.shape[1]
    partial_value = probe_product(matrix, test_matrix)
    own_rows = scatter_sum(partial_value, "col", n_col)
    sketch = gather_rows(own_rows, "col", n_col)
    width = k // n_col
    col = lax.axis_index("col")
    columns = lax.dynamic_slice_in_dim(sketch, col * width, width, 1)
    gram_part = jnp.dot(sketch.T, columns, precision=lax.Precision.HIGHEST) / jnp.float32(total_rows)
    gram_part = butterfly_sum(gram_part, "row", n_row)
    gram = gather_rows(gram_part.T, "col", n_col)
    share = own_rows.shape[0]
    extra = jnp.concatenate([own_rows.T, jnp.zeros((k, PANEL - share), jnp.float32)], axis=1)
    upper, solved = factor(gram, extra)
    return (solved[:, :share].T, upper)


def solution(mesh):
    in_specs = (P("row", "col"), P(("col", "row"), None))
    out_specs = (P(("row", "col"), None), P())
    return jax.shard_map(shards, mesh=mesh, in_specs=in_specs, out_specs=out_specs, check_vma=False)
```

```python
import jax
import jax.numpy as jnp
from jax import lax
from jax.experimental import pallas as pl
from jax.experimental.pallas import tpu as pltpu
from jax.sharding import PartitionSpec as P

PANEL = 128
GROUP = 32


def factor_kernel(a_ref, e_ref, r_ref, x_ref, w_ref, head_ref, row_ref):
    n = a_ref.shape[0]
    width = n + e_ref.shape[1]
    w_ref[:, :n] = a_ref[...]
    w_ref[:, n:] = e_ref[...]
    subl = lax.broadcasted_iota(jnp.int32, (GROUP, 1), 0)
    for k in range(n // PANEL):
        base = k * PANEL
        span = width - base
        lanes = lax.broadcasted_iota(jnp.int32, (1, span), 1) + base
        if base:
            r_ref[base:base + PANEL, :base] = jnp.zeros((PANEL, base), jnp.float32)
        for g in range(PANEL // GROUP):
            r0 = base + g * GROUP
            block = w_ref[r0:r0 + GROUP, base:]
            rows = jnp.zeros((GROUP, span), jnp.float32)
            for t in range(GROUP):
                j = r0 + t
                column = block[:, j - base:j - base + 1]
                pivot = column[t:t + 1, :]
                scale = lax.rsqrt(pivot)
                factor_col = jnp.where(subl > t, column * scale, 0.0)
                top = jnp.where(lanes >= j, block[t:t + 1, :] * scale, 0.0)
                rows = jnp.where(subl == t, top, rows)
                block = block - factor_col * top
            r_ref[r0:r0 + GROUP, base:] = rows[:, :n - base]
            x_ref[r0:r0 + GROUP, :] = rows[:, n - base:]
            below = r0 + GROUP - base
            if below < PANEL:
                head = jnp.transpose(rows[:, :PANEL])
                for t in range(GROUP):
                    row_ref[t, :, :span] = jnp.broadcast_to(rows[t:t + 1, :], (GROUP, span))
                    head_ref[t, below:, :] = jnp.broadcast_to(head[below:, t:t + 1], (PANEL - below, PANEL))
                for at in range(below, PANEL, GROUP):
                    part = w_ref[base + at:base + at + GROUP, base:]
                    for t in range(GROUP):
                        mult = head_ref[t, at:at + GROUP, :]
                        mult = jnp.concatenate([mult] * (span // PANEL), axis=1)
                        part = part - mult * row_ref[t, :, :span]
                    w_ref[base + at:base + at + GROUP, base:] = part
        rest = base + PANEL
        if rest < n:
            left = r_ref[base:rest, rest:]
            block = jnp.concatenate([left, x_ref[base:rest, :]], axis=1)
            left = jnp.transpose(left)
            update = jnp.dot(left, block, precision=lax.Precision.HIGHEST, preferred_element_type=jnp.float32)
            w_ref[rest:n, rest:] = w_ref[rest:n, rest:] - update


def factor(gram, extra):
    n, more = gram.shape[0], extra.shape[1]
    width = n + more
    return pl.pallas_call(
        factor_kernel,
        out_shape=(jax.ShapeDtypeStruct((n, n), jnp.float32), jax.ShapeDtypeStruct((n, more), jnp.float32)),
        in_specs=[pl.BlockSpec(memory_space=pltpu.VMEM)] * 2,
        out_specs=(pl.BlockSpec(memory_space=pltpu.VMEM),) * 2,
        scratch_shapes=[
            pltpu.VMEM((n, width), jnp.float32),
            pltpu.VMEM((GROUP, PANEL, PANEL), jnp.float32),
            pltpu.VMEM((GROUP, GROUP, width), jnp.float32),
        ],
    )(gram, extra)


def probe_product(matrix, test_matrix):
    return jnp.dot(
        matrix,
        lax.all_gather(test_matrix, "row", axis=0, tiled=True),
        preferred_element_type=jnp.float32,
    )


def scatter_sum(value, axis, parts):
    pieces = value.reshape(parts, value.shape[0] // parts, *value.shape[1:])
    return lax.all_to_all(pieces, axis, 0, 0, tiled=False).sum(0)


def gather_rows(value, axis, parts):
    copies = jnp.broadcast_to(value[None], (parts, *value.shape))
    gathered = lax.all_to_all(copies, axis, 0, 0, tiled=False)
    return gathered.reshape(parts * value.shape[0], *value.shape[1:])


def butterfly_sum(value, axis, parts):
    assert parts & (parts - 1) == 0
    distance = 1
    while distance < parts:
        value = value + lax.ppermute(value, axis, [(i, i ^ distance) for i in range(parts)])
        distance *= 2
    return value


def shards(matrix, test_matrix):
    n_col = lax.axis_size("col")
    n_row = lax.axis_size("row")
    total_rows = matrix.shape[0] * n_row
    k = test_matrix.shape[1]
    partial_value = probe_product(matrix, test_matrix)
    own_rows = scatter_sum(partial_value, "col", n_col)
    sketch = gather_rows(own_rows, "col", n_col)
    width = k // n_col
    col = lax.axis_index("col")
    columns = lax.dynamic_slice_in_dim(sketch, col * width, width, 1)
    gram_part = jnp.dot(sketch.T, columns, precision=lax.Precision.HIGHEST) / jnp.float32(total_rows)
    half = k // 2
    gram = jnp.concatenate(
        [gather_rows(butterfly_sum(gram_part[h:h + half], "row", n_row).T, "col", n_col) for h in (0, half)], axis=1
    )
    share = own_rows.shape[0]
    extra = jnp.concatenate([own_rows.T, jnp.zeros((k, PANEL - share), jnp.float32)], axis=1)
    upper, solved = factor(gram, extra)
    return (solved[:, :share].T, upper)


def solution(mesh):
    in_specs = (P("row", "col"), P(("col", "row"), None))
    out_specs = (P(("row", "col"), None), P())
    return jax.shard_map(shards, mesh=mesh, in_specs=in_specs, out_specs=out_specs, check_vma=False)
```

```python
import jax
import jax.numpy as jnp
from jax import lax
from jax.experimental import pallas as pl
from jax.experimental.pallas import tpu as pltpu
from jax.sharding import PartitionSpec as P

PANEL = 128
GROUP = 32


def factor_kernel(a_ref, e_ref, r_ref, out_ref, x_ref, w_ref, head_ref, row_ref):
    n = a_ref.shape[0]
    width = n + PANEL
    share = e_ref.shape[0]
    w_ref[:, :n] = a_ref[...]
    padded = jnp.concatenate([e_ref[...], jnp.zeros((PANEL - share, n), jnp.float32)], axis=0)
    w_ref[:, n:] = jnp.transpose(padded)
    subl = lax.broadcasted_iota(jnp.int32, (GROUP, 1), 0)
    for k in range(n // PANEL):
        base = k * PANEL
        span = width - base
        lanes = lax.broadcasted_iota(jnp.int32, (1, span), 1) + base
        if base:
            r_ref[base:base + PANEL, :base] = jnp.zeros((PANEL, base), jnp.float32)
        for g in range(PANEL // GROUP):
            r0 = base + g * GROUP
            block = w_ref[r0:r0 + GROUP, base:]
            rows = jnp.zeros((GROUP, span), jnp.float32)
            for t in range(GROUP):
                j = r0 + t
                column = block[:, j - base:j - base + 1]
                pivot = column[t:t + 1, :]
                scale = lax.rsqrt(pivot)
                factor_col = jnp.where(subl > t, column * scale, 0.0)
                top = jnp.where(lanes >= j, block[t:t + 1, :] * scale, 0.0)
                rows = jnp.where(subl == t, top, rows)
                block = block - factor_col * top
            r_ref[r0:r0 + GROUP, base:] = rows[:, :n - base]
            x_ref[r0:r0 + GROUP, :] = rows[:, n - base:]
            below = r0 + GROUP - base
            if below < PANEL:
                head = jnp.transpose(rows[:, :PANEL])
                for t in range(GROUP):
                    row_ref[t, :, :span] = jnp.broadcast_to(rows[t:t + 1, :], (GROUP, span))
                    head_ref[t, below:, :] = jnp.broadcast_to(head[below:, t:t + 1], (PANEL - below, PANEL))
                for at in range(below, PANEL, GROUP):
                    part = w_ref[base + at:base + at + GROUP, base:]
                    for t in range(GROUP):
                        mult = head_ref[t, at:at + GROUP, :]
                        mult = jnp.concatenate([mult] * (span // PANEL), axis=1)
                        part = part - mult * row_ref[t, :, :span]
                    w_ref[base + at:base + at + GROUP, base:] = part
        rest = base + PANEL
        if rest < n:
            left = r_ref[base:rest, rest:]
            block = jnp.concatenate([left, x_ref[base:rest, :]], axis=1)
            left = jnp.transpose(left)
            update = jnp.dot(left, block, precision=lax.Precision.HIGHEST, preferred_element_type=jnp.float32)
            w_ref[rest:n, rest:] = w_ref[rest:n, rest:] - update
    out_ref[...] = jnp.transpose(x_ref[...])[:share, :]


def factor(gram, extra):
    n, share = gram.shape[0], extra.shape[0]
    width = n + PANEL
    return pl.pallas_call(
        factor_kernel,
        out_shape=(jax.ShapeDtypeStruct((n, n), jnp.float32), jax.ShapeDtypeStruct((share, n), jnp.float32)),
        in_specs=[pl.BlockSpec(memory_space=pltpu.VMEM)] * 2,
        out_specs=(pl.BlockSpec(memory_space=pltpu.VMEM),) * 2,
        scratch_shapes=[
            pltpu.VMEM((n, PANEL), jnp.float32),
            pltpu.VMEM((n, width), jnp.float32),
            pltpu.VMEM((GROUP, PANEL, PANEL), jnp.float32),
            pltpu.VMEM((GROUP, GROUP, width), jnp.float32),
        ],
    )(gram, extra)


def probe_product(matrix, test_matrix):
    return jnp.dot(
        matrix,
        lax.all_gather(test_matrix, "row", axis=0, tiled=True),
        preferred_element_type=jnp.float32,
    )


def scatter_sum(value, axis, parts):
    pieces = value.reshape(parts, value.shape[0] // parts, *value.shape[1:])
    return lax.all_to_all(pieces, axis, 0, 0, tiled=False).sum(0)


def gather_rows(value, axis, parts):
    copies = jnp.broadcast_to(value[None], (parts, *value.shape))
    gathered = lax.all_to_all(copies, axis, 0, 0, tiled=False)
    return gathered.reshape(parts * value.shape[0], *value.shape[1:])


def butterfly_sum(value, axis, parts):
    assert parts & (parts - 1) == 0
    distance = 1
    while distance < parts:
        value = value + lax.ppermute(value, axis, [(i, i ^ distance) for i in range(parts)])
        distance *= 2
    return value


def shards(matrix, test_matrix):
    n_col = lax.axis_size("col")
    n_row = lax.axis_size("row")
    total_rows = matrix.shape[0] * n_row
    k = test_matrix.shape[1]
    partial_value = probe_product(matrix, test_matrix)
    own_rows = scatter_sum(partial_value, "col", n_col)
    sketch = gather_rows(own_rows, "col", n_col)
    width = k // n_col
    col = lax.axis_index("col")
    columns = lax.dynamic_slice_in_dim(sketch, col * width, width, 1)
    gram_part = jnp.dot(sketch.T, columns, precision=lax.Precision.HIGHEST) / jnp.float32(total_rows)
    gram_part = butterfly_sum(gram_part, "row", n_row)
    gram = gather_rows(gram_part.T, "col", n_col)
    upper, solved = factor(gram, own_rows)
    return (solved, upper)


def solution(mesh):
    in_specs = (P("row", "col"), P(("col", "row"), None))
    out_specs = (P(("row", "col"), None), P())
    return jax.shard_map(shards, mesh=mesh, in_specs=in_specs, out_specs=out_specs, check_vma=False)
```
